128 devices in a mesh: group: 4 (over z), member: 32 (over x, y, core).
Axes of the slice: x: 4, y: 4, z: 4, core: 2. Of those that a mesh axis runs over, the one named last changes fastest.
Arguments:
- passage_hidden: bfloat16 [16384, 768], P(('group', 'member')), may hold values from -6 to 6
- query_hidden: bfloat16 [65536, 768], P(('group', 'member')), may hold values from -96 to 96
- proj_weight: bfloat16 [768, 768], replicated, may hold values from -0.21875 to 0.21875
- cluster: int32 [16384], P(('group', 'member')), may hold values from 0 to 3, as said below
- place: int32 [16384], P(('group', 'member')), may hold values from 0 to 4095, as said below
- positive: int32 [65536], P(('group', 'member')), may hold values from 0 to 4095
- loss_weight: float32 [65536], P(('group', 'member')), may hold values from 8 to 64
Outputs:
- loss: float32 [65536], P(('group', 'member'))
- grad_query_hidden: bfloat16 [65536, 768], P(('group', 'member'))
- grad_passage_hidden: bfloat16 [16384, 768], P(('group', 'member'))
- grad_weight: float32 [768, 768], replicated
The draws below stay inside these ranges and needn't reach their ends.
Inputs may be any that keep to these rules, and one draw needn't show every extreme that they name: Every cluster group holds exactly 4096 passages. Within one cluster group each row 0 to 4095 is taken by exactly one passage. Call the owner of a passage the device cluster * 32 + place // 128; every device owns 128 passages, every device sends at most 2 passages to one owner and exactly 2 to some owner, and the count that device d sends to owner o depends only on o - d modulo 128.
All inputs are finite; a program needn't handle non-finite values.
Results may differ from the reference program's by a relative error of at most 0.0095.
Values may be sent and summed in bfloat16 or wider, within the bound.
No kernel may reach another device: no remote copies, remote signals or barrier semaphores. Data moves between devices by JAX's collectives and lax.ppermute only.
A program may use at most 128 MiB of HBM per device.

```python
import math
import jax
import jax.numpy as jnp
from jax import lax

D = 768
TOK_DEV = 128
Q_DEV = 512
DEVICE_COUNT = 128
PASSAGES = 16384
QUERIES = 65536
GROUP_ROWS = 4096
N_GROUP = 4
N_MEMBER = 32


def routing(key):
    devices = N_GROUP * N_MEMBER
    half = devices // 2
    base = jnp.arange(TOK_DEV, dtype=jnp.int32) % devices
    flips = jax.random.randint(jax.random.fold_in(key, 11), (half,), 0, 3).astype(jnp.int32)
    flips = flips.at[1].set(0).at[half - 1].set(0).at[0].set(2)
    lower = base < half
    pair_index = jnp.where(lower, base, base - half)
    flip_kind = flips[pair_index]
    moved = jnp.where(lower & (flip_kind == 2), base + half, base)
    moved = jnp.where(jnp.logical_not(lower) & (flip_kind == 1), base - half, moved)
    row_keys = jax.random.split(jax.random.fold_in(key, 12), devices)
    row_order = jax.vmap(lambda k: jax.random.permutation(k, TOK_DEV))(row_keys).astype(jnp.int32)
    offsets = moved[row_order]
    sources = jnp.arange(devices, dtype=jnp.int32)[:, None]
    owner = (sources + offsets) % devices
    slot_keys = jax.random.split(jax.random.fold_in(key, 13), devices)
    slot_table = jax.vmap(lambda k: jax.random.permutation(k, TOK_DEV))(slot_keys).astype(jnp.int32)
    slot = slot_table[owner, row_order]
    cluster = owner // N_MEMBER
    place = owner % N_MEMBER * TOK_DEV + slot
    return (cluster.reshape(-1).astype(jnp.int32), place.reshape(-1).astype(jnp.int32))


def positives(key):
    return jax.random.randint(jax.random.fold_in(key, 14), (QUERIES,), 0, GROUP_ROWS).astype(jnp.int32)


def hidden_pair(key):
    passages = jnp.clip(jax.random.normal(jax.random.fold_in(key, 21), (PASSAGES, D), jnp.float32), -6.0, 6.0)
    queries = jax.random.normal(jax.random.fold_in(key, 22), (QUERIES, D), jnp.float32)
    queries = jnp.clip(queries, -6.0, 6.0)
    return (passages, queries)


def draw_cluster(key, part):
    return routing(key)[0]


def draw_place(key, part):
    return routing(key)[1]


def draw_positive(key, part):
    return positives(key)


def draw_passage_hidden(key, part):
    return hidden_pair(key)[0].astype(jnp.bfloat16)


def draw_query_hidden(key, part):
    return hidden_pair(key)[1].astype(jnp.bfloat16)


def steps_of(stream_key, shape, pieces, low, largest):
    factor_of, own = 1.0, jax.random.fold_in(stream_key, 6)
    for position, shards_of in pieces:
        draws = jnp.exp(jax.random.uniform(jax.random.fold_in(own, position), (shards_of,), jnp.float32, low / len(pieces), largest / len(pieces)))
        factor_of = factor_of * jnp.repeat(draws, shape[position] // shards_of).reshape([-1 if axis == position else 1 for axis in range(len(shape))])
    return factor_of


def normal_values(own_key, extent, scale, limit, kind=jnp.bfloat16):
    values = scale * jax.random.normal(own_key, extent, jnp.float32)
    return jnp.clip(values, min=-limit, max=limit).astype(kind)


def setup_inputs(seed: int = 0) -> dict:
    key_list = jax.random.split(jax.random.key(seed), 8)
    return {
        "passage_hidden": draw_passage_hidden(jax.random.fold_in(key_list[7], 71), 0),
        "query_hidden": draw_query_hidden(jax.random.fold_in(key_list[7], 71), 0),
        "proj_weight": normal_values(key_list[2], (D, D), D ** -0.5, 0.21875),
        "cluster": draw_cluster(jax.random.fold_in(key_list[7], 71), 0),
        "place": draw_place(jax.random.fold_in(key_list[7], 71), 0),
        "positive": draw_positive(jax.random.fold_in(key_list[7], 71), 0),
        "loss_weight": jnp.clip(jnp.exp(math.log(64.0) - 2.0794415 * jax.random.uniform(key_list[6], (QUERIES,), jnp.float32) ** steps_of(key_list[6], (QUERIES,), ((0, 128),), -0.2, 0.2)), 8.0, 64.0),
    }


def reference(passage_hidden, query_hidden, proj_weight, cluster, place, positive, loss_weight):
    factor = 1.0 / math.sqrt(D)
    passage_emb = jnp.dot(passage_hidden, proj_weight, preferred_element_type=jnp.float32).astype(jnp.bfloat16)
    query_emb = jnp.dot(query_hidden, proj_weight, preferred_element_type=jnp.float32).astype(jnp.bfloat16)
    target = (cluster * GROUP_ROWS + place).astype(jnp.int32)
    relaid = jnp.zeros((PASSAGES, D), jnp.bfloat16).at[target].set(passage_emb)
    per_group = N_MEMBER * Q_DEV
    passages_grouped = relaid.reshape(N_GROUP, GROUP_ROWS, D)
    queries_grouped = query_emb.reshape(N_GROUP, per_group, D)
    positive_grouped = positive.reshape(N_GROUP, per_group)
    weight_grouped = loss_weight.reshape(N_GROUP, per_group)

    def one_group(items):
        keys, queries, targets, weights = items
        keys_wide = keys.astype(jnp.float32)
        queries_wide = queries.astype(jnp.float32)
        scores = jnp.dot(queries_wide, keys_wide.T) * factor
        top = lax.optimization_barrier(jnp.max(scores, axis=1, keepdims=True))
        lse = top[:, 0] + jnp.log(lax.optimization_barrier(jnp.sum(jnp.exp(scores - top), axis=1)))
        hit = jnp.arange(GROUP_ROWS, dtype=jnp.int32)[None, :] == targets[:, None]
        loss = lse - lax.optimization_barrier(jnp.sum(jnp.where(hit, scores, 0.0), axis=1))
        coef = (weights[:, None] * (jnp.exp(scores - lse[:, None]) - hit.astype(jnp.float32)) * factor).astype(jnp.bfloat16)
        coef_wide = coef.astype(jnp.float32)
        query_grad = jnp.dot(coef_wide, keys_wide).astype(jnp.bfloat16)
        relaid_grad = jnp.dot(coef_wide.T, queries_wide).astype(jnp.bfloat16)
        return (loss, query_grad, relaid_grad)
    loss, query_grad, relaid_grad = lax.map(one_group, (passages_grouped, queries_grouped, positive_grouped, weight_grouped))
    loss = loss.reshape(QUERIES)
    query_grad = query_grad.reshape(QUERIES, D)
    passage_grad = relaid_grad.reshape(PASSAGES, D)[target]
    grad_query_hidden = jnp.dot(query_grad, proj_weight.T, preferred_element_type=jnp.float32).astype(jnp.bfloat16)
    grad_passage_hidden = jnp.dot(passage_grad, proj_weight.T, preferred_element_type=jnp.float32).astype(jnp.bfloat16)
    grad_weight = (jnp.dot(passage_hidden.T, passage_grad, preferred_element_type=jnp.float32) + jnp.dot(query_hidden.T, query_grad, preferred_element_type=jnp.float32)) / DEVICE_COUNT
    return (loss, grad_query_hidden, grad_passage_hidden, grad_weight)
```

```python
import math

import jax
import jax.numpy as jnp
from jax import lax
from jax.sharding import PartitionSpec as P


def contract(left, right, left_dim, right_dim):
    return lax.dot_general(
        left, right, (((left_dim,), (right_dim,)), ((), ())), preferred_element_type=jnp.float32
    )


def shards(passage_hidden, query_hidden, proj_weight, cluster, place, positive, loss_weight):
    rows, width = passage_hidden.shape
    members = lax.axis_size("member")
    groups = lax.axis_size("group")
    devices = members * groups
    group_rows = rows * members
    capacity = 2 * rows // devices
    factor = 1.0 / math.sqrt(width)
    passage_emb = jnp.dot(passage_hidden, proj_weight, preferred_element_type=jnp.float32).astype(
        jnp.bfloat16
    )
    query_emb = jnp.dot(query_hidden, proj_weight, preferred_element_type=jnp.float32).astype(
        jnp.bfloat16
    )
    target = cluster * group_rows + place
    owner = target // rows
    slot = target % rows
    order = jnp.arange(rows, dtype=jnp.int32)
    earlier_same = (owner[:, None] == owner[None, :]) & (order[:, None] > order[None, :])
    rank = jnp.sum(earlier_same.astype(jnp.int32), axis=1)
    position = owner * capacity + rank
    both = jnp.concatenate([passage_emb, passage_hidden], axis=1)
    send_rows = jnp.zeros((devices * capacity, 2 * width), jnp.bfloat16).at[position].set(both)
    send_slots = jnp.full((devices * capacity,), rows, jnp.int32).at[position].set(slot)
    got_rows, got_slots = (
        lax.all_to_all(send_rows, ("group", "member"), split_axis=0, concat_axis=0, tiled=True),
        lax.all_to_all(send_slots, ("group", "member"), split_axis=0, concat_axis=0, tiled=True),
    )
    relaid = jnp.zeros((rows, 2 * width), jnp.bfloat16).at[got_slots].set(got_rows, mode="drop")
    group_both = lax.all_gather(relaid, "member", axis=0, tiled=True)
    group_passages = group_both[:, :width]
    group_hidden = group_both[:, width:]
    scores = contract(query_emb, group_passages, 1, 1) * factor
    top = jnp.max(scores, axis=1, keepdims=True)
    lse = top[:, 0] + jnp.log(jnp.sum(jnp.exp(scores - top), axis=1))
    hit = jnp.arange(group_rows, dtype=jnp.int32)[None, :] == positive[:, None]
    loss = lse - jnp.sum(jnp.where(hit, scores, 0.0), axis=1)
    coef = (
        loss_weight[:, None] * (jnp.exp(scores - lse[:, None]) - hit.astype(jnp.float32)) * factor
    ).astype(jnp.bfloat16)
    query_grad = jnp.dot(coef, group_passages, preferred_element_type=jnp.float32).astype(
        jnp.bfloat16
    )
    partial = contract(coef, query_emb, 0, 0)
    local_weight = contract(query_hidden, query_grad, 0, 0) + contract(group_hidden, partial, 0, 0)
    grad_weight = lax.psum(local_weight, ("group", "member")) / devices
    pieces = lax.all_to_all(
        partial.astype(jnp.bfloat16).reshape(members, rows, width),
        "member",
        split_axis=0,
        concat_axis=0,
        tiled=True,
    )
    relaid_grad = jnp.sum(pieces.astype(jnp.float32), axis=0).astype(jnp.bfloat16)
    back_rows = relaid_grad[jnp.minimum(got_slots, rows - 1)]
    returned = lax.all_to_all(
        back_rows, ("group", "member"), split_axis=0, concat_axis=0, tiled=True
    )
    passage_grad = returned[position]
    grad_passage_hidden = contract(passage_grad, proj_weight, 1, 1).astype(jnp.bfloat16)
    grad_query_hidden = contract(query_grad, proj_weight, 1, 1).astype(jnp.bfloat16)
    return (loss, grad_query_hidden, grad_passage_hidden, grad_weight)


def solution(mesh):
    in_specs = (
        P(("group", "member"), None),
        P(("group", "member"), None),
        P(),
        P(("group", "member")),
        P(("group", "member")),
        P(("group", "member")),
        P(("group", "member")),
    )
    out_specs = (
        P(("group", "member")),
        P(("group", "member"), None),
        P(("group", "member"), None),
        P(),
    )
    return jax.shard_map(shards, mesh=mesh, in_specs=in_specs, out_specs=out_specs, check_vma=False)
```

```python
import math

import jax
import jax.numpy as jnp
from jax import lax
from jax.sharding import PartitionSpec as P


def contract(left, right, left_dim, right_dim):
    return lax.dot_general(
        left, right, (((left_dim,), (right_dim,)), ((), ())), preferred_element_type=jnp.float32
    )


def shards(passage_hidden, query_hidden, proj_weight, cluster, place, positive, loss_weight):
    rows, width = passage_hidden.shape
    members = lax.axis_size("member")
    groups = lax.axis_size("group")
    devices = members * groups
    group_rows = rows * members
    capacity = 2 * rows // devices
    factor = 1.0 / math.sqrt(width)
    passage_emb = jnp.dot(passage_hidden, proj_weight, preferred_element_type=jnp.float32).astype(
        jnp.bfloat16
    )
    query_emb = jnp.dot(query_hidden, proj_weight, preferred_element_type=jnp.float32).astype(
        jnp.bfloat16
    )
    target = cluster * group_rows + place
    owner = target // rows
    slot = target % rows
    order = jnp.arange(rows, dtype=jnp.int32)
    earlier_same = (owner[:, None] == owner[None, :]) & (order[:, None] > order[None, :])
    rank = jnp.sum(earlier_same.astype(jnp.int32), axis=1)
    position = owner * capacity + rank
    both = jnp.concatenate([passage_emb, passage_hidden], axis=1)
    send_rows = jnp.zeros((devices * capacity, 2 * width), jnp.bfloat16).at[position].set(both)
    send_slots = jnp.full((devices * capacity,), rows, jnp.int32).at[position].set(slot)
    got_rows, got_slots = (
        lax.all_to_all(send_rows, ("group", "member"), split_axis=0, concat_axis=0, tiled=True),
        lax.all_to_all(send_slots, ("group", "member"), split_axis=0, concat_axis=0, tiled=True),
    )
    relaid = jnp.zeros((rows, 2 * width), jnp.bfloat16).at[got_slots].set(got_rows, mode="drop")
    group_both = lax.all_gather(relaid, "member", axis=0, tiled=True)
    group_passages = group_both[:, :width]
    group_hidden = group_both[:, width:]
    scores = contract(query_emb, group_passages, 1, 1) * factor
    top = jnp.max(scores, axis=1, keepdims=True)
    lse = top[:, 0] + jnp.log(jnp.sum(jnp.exp(scores - top), axis=1))
    hit = jnp.arange(group_rows, dtype=jnp.int32)[None, :] == positive[:, None]
    loss = lse - jnp.sum(jnp.where(hit, scores, 0.0), axis=1)
    coef = (
        loss_weight[:, None] * (jnp.exp(scores - lse[:, None]) - hit.astype(jnp.float32)) * factor
    ).astype(jnp.bfloat16)
    query_grad = jnp.dot(coef, group_passages, preferred_element_type=jnp.float32).astype(
        jnp.bfloat16
    )
    partial = contract(coef, query_emb, 0, 0)
    local_weight = contract(query_hidden, query_grad, 0, 0) + contract(group_hidden, partial, 0, 0)
    weight_rows = width // members
    weight_pieces = lax.all_to_all(
        local_weight.reshape(members, weight_rows, width), "member", 0, 0, tiled=True
    )
    weight_share = lax.psum(jnp.sum(weight_pieces, axis=0), "group")
    grad_weight = lax.all_gather(weight_share, "member", axis=0, tiled=True) / devices
    pieces = lax.all_to_all(
        partial.astype(jnp.bfloat16).reshape(members, rows, width),
        "member",
        split_axis=0,
        concat_axis=0,
        tiled=True,
    )
    relaid_grad = jnp.sum(pieces.astype(jnp.float32), axis=0).astype(jnp.bfloat16)
    back_rows = relaid_grad[jnp.minimum(got_slots, rows - 1)]
    returned = lax.all_to_all(
        back_rows, ("group", "member"), split_axis=0, concat_axis=0, tiled=True
    )
    passage_grad = returned[position]
    grad_passage_hidden = contract(passage_grad, proj_weight, 1, 1).astype(jnp.bfloat16)
    grad_query_hidden = contract(query_grad, proj_weight, 1, 1).astype(jnp.bfloat16)
    return (loss, grad_query_hidden, grad_passage_hidden, grad_weight)


def solution(mesh):
    in_specs = (
        P(("group", "member"), None),
        P(("group", "member"), None),
        P(),
        P(("group", "member")),
        P(("group", "member")),
        P(("group", "member")),
        P(("group", "member")),
    )
    out_specs = (
        P(("group", "member")),
        P(("group", "member"), None),
        P(("group", "member"), None),
        P(),
    )
    return jax.shard_map(shards, mesh=mesh, in_specs=in_specs, out_specs=out_specs, check_vma=False)
```

```python
import math

import jax
import jax.numpy as jnp
from jax import lax
from jax.sharding import PartitionSpec as P


def contract(left, right, left_dim, right_dim):
    return lax.dot_general(
        left, right, (((left_dim,), (right_dim,)), ((), ())), preferred_element_type=jnp.float32
    )


def shards(passage_hidden, query_hidden, proj_weight, cluster, place, positive, loss_weight):
    rows, width = passage_hidden.shape
    members = lax.axis_size("member")
    groups = lax.axis_size("group")
    devices = members * groups
    group_rows = rows * members
    capacity = 2 * rows // devices
    factor = 1.0 / math.sqrt(width)
    passage_emb = jnp.dot(passage_hidden, proj_weight, preferred_element_type=jnp.float32).astype(
        jnp.bfloat16
    )
    query_emb = jnp.dot(query_hidden, proj_weight, preferred_element_type=jnp.float32).astype(
        jnp.bfloat16
    )
    target = cluster * group_rows + place
    owner = target // rows
    slot = target % rows
    order = jnp.arange(rows, dtype=jnp.int32)
    earlier_same = (owner[:, None] == owner[None, :]) & (order[:, None] > order[None, :])
    rank = jnp.sum(earlier_same.astype(jnp.int32), axis=1)
    position = owner * capacity + rank
    both = jnp.concatenate([passage_emb, passage_hidden], axis=1)
    send_rows = jnp.zeros((devices * capacity, 2 * width), jnp.bfloat16).at[position].set(both)
    send_slots = jnp.full((devices * capacity,), rows, jnp.int32).at[position].set(slot)
    got_rows, got_slots = (
        lax.all_to_all(send_rows, ("group", "member"), split_axis=0, concat_axis=0, tiled=True),
        lax.all_to_all(send_slots, ("group", "member"), split_axis=0, concat_axis=0, tiled=True),
    )
    relaid = jnp.zeros((rows, 2 * width), jnp.bfloat16).at[got_slots].set(got_rows, mode="drop")
    group_both = lax.all_gather(relaid, "member", axis=0, tiled=True)
    group_passages = group_both[:, :width]
    group_hidden = group_both[:, width:]
    scores = contract(query_emb, group_passages, 1, 1) * factor
    top = jnp.max(scores, axis=1, keepdims=True)
    lse = top[:, 0] + jnp.log(jnp.sum(jnp.exp(scores - top), axis=1))
    hit = jnp.arange(group_rows, dtype=jnp.int32)[None, :] == positive[:, None]
    loss = lse - jnp.sum(jnp.where(hit, scores, 0.0), axis=1)
    coef = (
        loss_weight[:, None] * (jnp.exp(scores - lse[:, None]) - hit.astype(jnp.float32)) * factor
    ).astype(jnp.bfloat16)
    query_grad = jnp.dot(coef, group_passages, preferred_element_type=jnp.float32).astype(
        jnp.bfloat16
    )
    partial = contract(coef, query_emb, 0, 0)
    local_weight = contract(query_hidden, query_grad, 0, 0) + contract(group_hidden, partial, 0, 0)
    weight_share = lax.psum(
        lax.psum_scatter(local_weight, "member", scatter_dimension=0, tiled=True), "group"
    )
    grad_weight = lax.all_gather(weight_share, "member", axis=0, tiled=True) / devices
    pieces = lax.all_to_all(
        partial.astype(jnp.bfloat16).reshape(members, rows, width),
        "member",
        split_axis=0,
        concat_axis=0,
        tiled=True,
    )
    relaid_grad = jnp.sum(pieces.astype(jnp.float32), axis=0).astype(jnp.bfloat16)
    back_rows = relaid_grad[jnp.minimum(got_slots, rows - 1)]
    returned = lax.all_to_all(
        back_rows, ("group", "member"), split_axis=0, concat_axis=0, tiled=True
    )
    passage_grad = returned[position]
    grad_passage_hidden = contract(passage_grad, proj_weight, 1, 1).astype(jnp.bfloat16)
    grad_query_hidden = contract(query_grad, proj_weight, 1, 1).astype(jnp.bfloat16)
    return (loss, grad_query_hidden, grad_passage_hidden, grad_weight)


def solution(mesh):
    in_specs = (
        P(("group", "member"), None),
        P(("group", "member"), None),
        P(),
        P(("group", "member")),
        P(("group", "member")),
        P(("group", "member")),
        P(("group", "member")),
    )
    out_specs = (
        P(("group", "member")),
        P(("group", "member"), None),
        P(("group", "member"), None),
        P(),
    )
    return jax.shard_map(shards, mesh=mesh, in_specs=in_specs, out_specs=out_specs, check_vma=False)
```

```python
import math

import jax
import jax.numpy as jnp
from jax import lax
from jax.sharding import PartitionSpec as P


def contract(left, right, left_dim, right_dim):
    return lax.dot_general(
        left, right, (((left_dim,), (right_dim,)), ((), ())), preferred_element_type=jnp.float32
    )


def shards(passage_hidden, query_hidden, proj_weight, cluster, place, positive, loss_weight):
    rows, width = passage_hidden.shape
    members = lax.axis_size("member")
    groups = lax.axis_size("group")
    devices = members * groups
    group_rows = rows * members
    capacity = 2 * rows // devices
    factor = 1.0 / math.sqrt(width)
    passage_emb = jnp.dot(passage_hidden, proj_weight, preferred_element_type=jnp.float32).astype(
        jnp.bfloat16
    )
    query_emb = jnp.dot(query_hidden, proj_weight, preferred_element_type=jnp.float32).astype(
        jnp.bfloat16
    )
    target = cluster * group_rows + place
    owner = target // rows
    slot = target % rows
    order = jnp.arange(rows, dtype=jnp.int32)
    earlier_same = (owner[:, None] == owner[None, :]) & (order[:, None] > order[None, :])
    rank = jnp.sum(earlier_same.astype(jnp.int32), axis=1)
    position = owner * capacity + rank
    tag_width = 128
    tag = jnp.broadcast_to(slot.astype(jnp.bfloat16)[:, None], (rows, tag_width))
    both = jnp.concatenate([passage_emb, passage_hidden, tag], axis=1)
    send_rows = jnp.zeros((devices * capacity, 2 * width + tag_width), jnp.bfloat16)
    send_rows = send_rows.at[:, 2 * width :].set(rows).at[position].set(both)
    got = lax.all_to_all(send_rows, ("group", "member"), split_axis=0, concat_axis=0, tiled=True)
    got_rows = got[:, : 2 * width]
    got_slots = got[:, 2 * width].astype(jnp.int32)
    relaid = jnp.zeros((rows, 2 * width), jnp.bfloat16).at[got_slots].set(got_rows, mode="drop")
    group_both = lax.all_gather(relaid, "member", axis=0, tiled=True)
    group_passages = group_both[:, :width]
    group_hidden = group_both[:, width:]
    scores = contract(query_emb, group_passages, 1, 1) * factor
    top = jnp.max(scores, axis=1, keepdims=True)
    lse = top[:, 0] + jnp.log(jnp.sum(jnp.exp(scores - top), axis=1))
    hit = jnp.arange(group_rows, dtype=jnp.int32)[None, :] == positive[:, None]
    loss = lse - jnp.sum(jnp.where(hit, scores, 0.0), axis=1)
    coef = (
        loss_weight[:, None] * (jnp.exp(scores - lse[:, None]) - hit.astype(jnp.float32)) * factor
    ).astype(jnp.bfloat16)
    query_grad = jnp.dot(coef, group_passages, preferred_element_type=jnp.float32).astype(
        jnp.bfloat16
    )
    partial = contract(coef, query_emb, 0, 0)
    local_weight = contract(query_hidden, query_grad, 0, 0) + contract(group_hidden, partial, 0, 0)
    weight_rows = width // members
    weight_pieces = lax.all_to_all(
        local_weight.reshape(members, weight_rows, width), "member", 0, 0, tiled=True
    )
    weight_share = lax.psum(jnp.sum(weight_pieces, axis=0), "group")
    grad_weight = lax.all_gather(weight_share, "member", axis=0, tiled=True) / devices
    pieces = lax.all_to_all(
        partial.astype(jnp.bfloat16).reshape(members, rows, width),
        "member",
        split_axis=0,
        concat_axis=0,
        tiled=True,
    )
    relaid_grad = jnp.sum(pieces.astype(jnp.float32), axis=0).astype(jnp.bfloat16)
    back_rows = relaid_grad[jnp.minimum(got_slots, rows - 1)]
    returned = lax.all_to_all(
        back_rows, ("group", "member"), split_axis=0, concat_axis=0, tiled=True
    )
    passage_grad = returned[position]
    grad_passage_hidden = contract(passage_grad, proj_weight, 1, 1).astype(jnp.bfloat16)
    grad_query_hidden = contract(query_grad, proj_weight, 1, 1).astype(jnp.bfloat16)
    return (loss, grad_query_hidden, grad_passage_hidden, grad_weight)


def solution(mesh):
    in_specs = (
        P(("group", "member"), None),
        P(("group", "member"), None),
        P(),
        P(("group", "member")),
        P(("group", "member")),
        P(("group", "member")),
        P(("group", "member")),
    )
    out_specs = (
        P(("group", "member")),
        P(("group", "member"), None),
        P(("group", "member"), None),
        P(),
    )
    return jax.shard_map(shards, mesh=mesh, in_specs=in_specs, out_specs=out_specs, check_vma=False)
```

```python
import math

import jax
import jax.numpy as jnp
from jax import lax
from jax.sharding import PartitionSpec as P


def contract(left, right, left_dim, right_dim):
    return lax.dot_general(
        left, right, (((left_dim,), (right_dim,)), ((), ())), preferred_element_type=jnp.float32
    )


def body(passage_hidden, query_hidden, proj_weight, cluster, place, positive, loss_weight):
    rows, width = passage_hidden.shape
    members = lax.axis_size("member")
    groups = lax.axis_size("group")
    devices = members * groups
    group_rows = rows * members
    capacity = 2 * rows // devices
    factor = 1.0 / math.sqrt(width)
    passage_emb = jnp.dot(passage_hidden, proj_weight, preferred_element_type=jnp.float32).astype(
        jnp.bfloat16
    )
    query_emb = jnp.dot(query_hidden, proj_weight, preferred_element_type=jnp.float32).astype(
        jnp.bfloat16
    )
    target = cluster * group_rows + place
    owner = target // rows
    slot = target % rows
    order = jnp.arange(rows, dtype=jnp.int32)
    earlier_same = (owner[:, None] == owner[None, :]) & (order[:, None] > order[None, :])
    rank = jnp.sum(earlier_same.astype(jnp.int32), axis=1)
    position = owner * capacity + rank
    tag_width = 128
    tag = jnp.broadcast_to(slot.astype(jnp.bfloat16)[:, None], (rows, tag_width))
    both = jnp.concatenate([passage_emb, passage_hidden, tag], axis=1)
    send_rows = jnp.zeros((devices * capacity, 2 * width + tag_width), jnp.bfloat16)
    send_rows = send_rows.at[:, 2 * width :].set(rows).at[position].set(both)
    got = lax.all_to_all(send_rows, ("group", "member"), split_axis=0, concat_axis=0, tiled=True)
    got_rows = got[:, : 2 * width]
    got_slots = got[:, 2 * width].astype(jnp.int32)
    relaid = jnp.zeros((rows, 2 * width), jnp.bfloat16).at[got_slots].set(got_rows, mode="drop")
    group_both = lax.all_gather(relaid, "member", axis=0, tiled=True)
    group_passages = group_both[:, :width]
    group_hidden = group_both[:, width:]
    scores = contract(query_emb, group_passages, 1, 1) * factor
    top = jnp.max(scores, axis=1, keepdims=True)
    lse = top[:, 0] + jnp.log(jnp.sum(jnp.exp(scores - top), axis=1))
    hit = jnp.arange(group_rows, dtype=jnp.int32)[None, :] == positive[:, None]
    loss = lse - jnp.sum(jnp.where(hit, scores, 0.0), axis=1)
    coef = (
        loss_weight[:, None] * (jnp.exp(scores - lse[:, None]) - hit.astype(jnp.float32)) * factor
    ).astype(jnp.bfloat16)
    query_grad = jnp.dot(coef, group_passages, preferred_element_type=jnp.float32).astype(
        jnp.bfloat16
    )
    partial = contract(coef, query_emb, 0, 0)
    local_weight = contract(query_hidden, query_grad, 0, 0) + contract(group_hidden, partial, 0, 0)
    weight_rows = width // members
    weight_pieces = lax.all_to_all(
        local_weight.reshape(members, weight_rows, width), "member", 0, 0, tiled=True
    )
    weight_share = jnp.sum(weight_pieces, axis=0)
    step = 1
    while step < groups:
        pairs = [(index, index ^ step) for index in range(groups)]
        weight_share = weight_share + lax.ppermute(weight_share, "group", pairs)
        step *= 2
    grad_weight = lax.all_gather(weight_share, "member", axis=0, tiled=True) / devices
    pieces = lax.all_to_all(
        partial.astype(jnp.bfloat16).reshape(members, rows, width),
        "member",
        split_axis=0,
        concat_axis=0,
        tiled=True,
    )
    relaid_grad = jnp.sum(pieces.astype(jnp.float32), axis=0).astype(jnp.bfloat16)
    back_rows = relaid_grad[jnp.minimum(got_slots, rows - 1)]
    returned = lax.all_to_all(
        back_rows, ("group", "member"), split_axis=0, concat_axis=0, tiled=True
    )
    passage_grad = returned[position]
    grad_passage_hidden = contract(passage_grad, proj_weight, 1, 1).astype(jnp.bfloat16)
    grad_query_hidden = contract(query_grad, proj_weight, 1, 1).astype(jnp.bfloat16)
    return (loss, grad_query_hidden, grad_passage_hidden, grad_weight)


def solution(mesh):
    in_specs = (
        P(("group", "member"), None),
        P(("group", "member"), None),
        P(),
        P(("group", "member")),
        P(("group", "member")),
        P(("group", "member")),
        P(("group", "member")),
    )
    out_specs = (
        P(("group", "member")),
        P(("group", "member"), None),
        P(("group", "member"), None),
        P(),
    )
    return jax.shard_map(body, mesh=mesh, in_specs=in_specs, out_specs=out_specs, check_vma=False)
```

```python
import math

import jax
import jax.numpy as jnp
from jax import lax
from jax.sharding import PartitionSpec as P


MEMBER = ("chip", "core")
ALL = ("group", "chip", "core")


def contract(left, right, left_dim, right_dim):
    return lax.dot_general(
        left, right, (((left_dim,), (right_dim,)), ((), ())), preferred_element_type=jnp.float32
    )


def body(passage_hidden, query_hidden, proj_weight, cluster, place, positive, loss_weight):
    rows, width = passage_hidden.shape
    members = lax.axis_size("chip") * lax.axis_size("core")
    groups = lax.axis_size("group")
    devices = members * groups
    group_rows = rows * members
    capacity = 2 * rows // devices
    factor = 1.0 / math.sqrt(width)
    passage_emb = jnp.dot(passage_hidden, proj_weight, preferred_element_type=jnp.float32).astype(
        jnp.bfloat16
    )
    query_emb = jnp.dot(query_hidden, proj_weight, preferred_element_type=jnp.float32).astype(
        jnp.bfloat16
    )
    target = cluster * group_rows + place
    owner = target // rows
    slot = target % rows
    order = jnp.arange(rows, dtype=jnp.int32)
    earlier_same = (owner[:, None] == owner[None, :]) & (order[:, None] > order[None, :])
    rank = jnp.sum(earlier_same.astype(jnp.int32), axis=1)
    position = owner * capacity + rank
    tag_width = 128
    tag = jnp.broadcast_to(slot.astype(jnp.bfloat16)[:, None], (rows, tag_width))
    both = jnp.concatenate([passage_emb, passage_hidden, tag], axis=1)
    send_rows = jnp.zeros((devices * capacity, 2 * width + tag_width), jnp.bfloat16)
    send_rows = send_rows.at[:, 2 * width :].set(rows).at[position].set(both)
    got = lax.all_to_all(send_rows, ALL, split_axis=0, concat_axis=0, tiled=True)
    got_rows = got[:, : 2 * width]
    got_slots = got[:, 2 * width].astype(jnp.int32)
    relaid = jnp.zeros((rows, 2 * width), jnp.bfloat16).at[got_slots].set(got_rows, mode="drop")
    group_both = lax.all_gather(relaid, MEMBER, axis=0, tiled=True)
    group_passages = group_both[:, :width]
    group_hidden = group_both[:, width:]
    scores = contract(query_emb, group_passages, 1, 1) * factor
    top = jnp.max(scores, axis=1, keepdims=True)
    lse = top[:, 0] + jnp.log(jnp.sum(jnp.exp(scores - top), axis=1))
    hit = jnp.arange(group_rows, dtype=jnp.int32)[None, :] == positive[:, None]
    loss = lse - jnp.sum(jnp.where(hit, scores, 0.0), axis=1)
    coef = (
        loss_weight[:, None] * (jnp.exp(scores - lse[:, None]) - hit.astype(jnp.float32)) * factor
    ).astype(jnp.bfloat16)
    query_grad = jnp.dot(coef, group_passages, preferred_element_type=jnp.float32).astype(
        jnp.bfloat16
    )
    partial = contract(coef, query_emb, 0, 0)
    local_weight = contract(query_hidden, query_grad, 0, 0) + contract(group_hidden, partial, 0, 0)
    weight_rows = width // members
    weight_pieces = lax.all_to_all(
        local_weight.reshape(members, weight_rows, width), MEMBER, 0, 0, tiled=True
    )
    weight_share = jnp.sum(weight_pieces, axis=0)
    step = 1
    while step < groups:
        pairs = [(index, index ^ step) for index in range(groups)]
        weight_share = weight_share + lax.ppermute(weight_share, "group", pairs)
        step *= 2
    grad_weight = lax.all_gather(weight_share, MEMBER, axis=0, tiled=True) / devices
    chips = lax.axis_size("chip")
    core = lax.axis_index("core")
    split = partial.reshape(chips, 2, rows, width)
    kept = jnp.where(core == 0, split[:, 0], split[:, 1])
    given = jnp.where(core == 0, split[:, 1], split[:, 0]).astype(jnp.bfloat16)
    paired = kept + lax.ppermute(given, "core", [(0, 1), (1, 0)]).astype(jnp.float32)
    pieces = lax.all_to_all(
        paired.astype(jnp.bfloat16), "chip", split_axis=0, concat_axis=0, tiled=True
    )
    relaid_grad = jnp.sum(pieces.astype(jnp.float32), axis=0).astype(jnp.bfloat16)
    back_rows = relaid_grad[jnp.minimum(got_slots, rows - 1)]
    returned = lax.all_to_all(
        back_rows, ALL, split_axis=0, concat_axis=0, tiled=True
    )
    passage_grad = returned[position]
    grad_passage_hidden = contract(passage_grad, proj_weight, 1, 1).astype(jnp.bfloat16)
    grad_query_hidden = contract(query_grad, proj_weight, 1, 1).astype(jnp.bfloat16)
    return (loss, grad_query_hidden, grad_passage_hidden, grad_weight)


def solution(mesh):
    groups, members = mesh.devices.shape
    mesh = jax.sharding.Mesh(
        mesh.devices.reshape(groups, members // 2, 2), ("group", "chip", "core")
    )
    in_specs = (
        P(("group", "chip", "core"), None),
        P(("group", "chip", "core"), None),
        P(),
        P(("group", "chip", "core")),
        P(("group", "chip", "core")),
        P(("group", "chip", "core")),
        P(("group", "chip", "core")),
    )
    out_specs = (
        P(("group", "chip", "core")),
        P(("group", "chip", "core"), None),
        P(("group", "chip", "core"), None),
        P(),
    )
    return jax.shard_map(body, mesh=mesh, in_specs=in_specs, out_specs=out_specs, check_vma=False)
```

```python
import math

import jax
import jax.numpy as jnp
from jax import lax
from jax.sharding import PartitionSpec as P


MEMBER = ("chip", "core")
ALL = ("group", "chip", "core")


def contract(left, right, left_dim, right_dim):
    return lax.dot_general(
        left, right, (((left_dim,), (right_dim,)), ((), ())), preferred_element_type=jnp.float32
    )


def body(passage_hidden, query_hidden, proj_weight, cluster, place, positive, loss_weight):
    rows, width = passage_hidden.shape
    members = lax.axis_size("chip") * lax.axis_size("core")
    groups = lax.axis_size("group")
    devices = members * groups
    group_rows = rows * members
    capacity = 2 * rows // devices
    factor = 1.0 / math.sqrt(width)
    passage_emb = jnp.dot(passage_hidden, proj_weight, preferred_element_type=jnp.float32).astype(
        jnp.bfloat16
    )
    query_emb = jnp.dot(query_hidden, proj_weight, preferred_element_type=jnp.float32).astype(
        jnp.bfloat16
    )
    target = cluster * group_rows + place
    owner = target // rows
    slot = target % rows
    order = jnp.arange(rows, dtype=jnp.int32)
    earlier_same = (owner[:, None] == owner[None, :]) & (order[:, None] > order[None, :])
    rank = jnp.sum(earlier_same.astype(jnp.int32), axis=1)
    position = owner * capacity + rank
    tag_width = 128
    tag = jnp.broadcast_to(slot.astype(jnp.bfloat16)[:, None], (rows, tag_width))
    both = jnp.concatenate([passage_emb, passage_hidden, tag], axis=1)
    send_rows = jnp.zeros((devices * capacity, 2 * width + tag_width), jnp.bfloat16)
    send_rows = send_rows.at[:, 2 * width :].set(rows).at[position].set(both)
    got = lax.all_to_all(send_rows, ALL, split_axis=0, concat_axis=0, tiled=True)
    got_rows = got[:, : 2 * width]
    got_slots = got[:, 2 * width].astype(jnp.int32)
    relaid = jnp.zeros((rows, 2 * width), jnp.bfloat16).at[got_slots].set(got_rows, mode="drop")
    chips = lax.axis_size("chip")
    core = lax.axis_index("core")
    swap = [(0, 1), (1, 0)]
    chip_both = lax.all_gather(relaid, "chip", axis=0, tiled=True)
    group_both = jnp.concatenate([chip_both, lax.ppermute(chip_both, "core", swap)], axis=0)
    half = chips * rows
    positive_member = positive // rows
    positive = (
        jnp.where(positive_member % 2 == core, 0, half)
        + positive_member // 2 * rows
        + positive % rows
    )
    group_passages = group_both[:, :width]
    group_hidden = group_both[:, width:]
    scores = contract(query_emb, group_passages, 1, 1) * factor
    top = jnp.max(scores, axis=1, keepdims=True)
    lse = top[:, 0] + jnp.log(jnp.sum(jnp.exp(scores - top), axis=1))
    hit = jnp.arange(group_rows, dtype=jnp.int32)[None, :] == positive[:, None]
    loss = lse - jnp.sum(jnp.where(hit, scores, 0.0), axis=1)
    coef = (
        loss_weight[:, None] * (jnp.exp(scores - lse[:, None]) - hit.astype(jnp.float32)) * factor
    ).astype(jnp.bfloat16)
    query_grad = jnp.dot(coef, group_passages, preferred_element_type=jnp.float32).astype(
        jnp.bfloat16
    )
    partial = contract(coef, query_emb, 0, 0)
    local_weight = contract(query_hidden, query_grad, 0, 0) + contract(group_hidden, partial, 0, 0)
    weight_rows = width // members
    weight_split = local_weight.reshape(chips, 2, weight_rows, width)
    weight_kept = jnp.where(core == 0, weight_split[:, 0], weight_split[:, 1])
    weight_given = jnp.where(core == 0, weight_split[:, 1], weight_split[:, 0])
    weight_paired = weight_kept + lax.ppermute(weight_given, "core", swap)
    weight_pieces = lax.all_to_all(weight_paired, "chip", 0, 0, tiled=True)
    weight_share = jnp.sum(weight_pieces, axis=0)
    step = 1
    while step < groups:
        pairs = [(index, index ^ step) for index in range(groups)]
        weight_share = weight_share + lax.ppermute(weight_share, "group", pairs)
        step *= 2
    grad_weight = lax.all_gather(weight_share, MEMBER, axis=0, tiled=True) / devices
    kept = partial[:half].reshape(chips, rows, width)
    given = partial[half:].reshape(chips, rows, width).astype(jnp.bfloat16)
    paired = kept + lax.ppermute(given, "core", swap).astype(jnp.float32)
    pieces = lax.all_to_all(
        paired.astype(jnp.bfloat16), "chip", split_axis=0, concat_axis=0, tiled=True
    )
    relaid_grad = jnp.sum(pieces.astype(jnp.float32), axis=0).astype(jnp.bfloat16)
    back_rows = relaid_grad[jnp.minimum(got_slots, rows - 1)]
    returned = lax.all_to_all(
        back_rows, ALL, split_axis=0, concat_axis=0, tiled=True
    )
    passage_grad = returned[position]
    grad_passage_hidden = contract(passage_grad, proj_weight, 1, 1).astype(jnp.bfloat16)
    grad_query_hidden = contract(query_grad, proj_weight, 1, 1).astype(jnp.bfloat16)
    return (loss, grad_query_hidden, grad_passage_hidden, grad_weight)


def solution(mesh):
    groups, members = mesh.devices.shape
    mesh = jax.sharding.Mesh(
        mesh.devices.reshape(groups, members // 2, 2), ("group", "chip", "core")
    )
    in_specs = (
        P(("group", "chip", "core"), None),
        P(("group", "chip", "core"), None),
        P(),
        P(("group", "chip", "core")),
        P(("group", "chip", "core")),
        P(("group", "chip", "core")),
        P(("group", "chip", "core")),
    )
    out_specs = (
        P(("group", "chip", "core")),
        P(("group", "chip", "core"), None),
        P(("group", "chip", "core"), None),
        P(),
    )
    return jax.shard_map(body, mesh=mesh, in_specs=in_specs, out_specs=out_specs, check_vma=False)
```

```python
import math

import jax
import jax.numpy as jnp
from jax import lax
from jax.sharding import PartitionSpec as P


MEMBER = ("chip", "core")
ALL = ("group", "chip", "core")


def contract(left, right, left_dim, right_dim):
    return lax.dot_general(
        left, right, (((left_dim,), (right_dim,)), ((), ())), preferred_element_type=jnp.float32
    )


def body(passage_hidden, query_hidden, proj_weight, cluster, place, positive, loss_weight):
    rows, width = passage_hidden.shape
    members = lax.axis_size("chip") * lax.axis_size("core")
    groups = lax.axis_size("group")
    devices = members * groups
    group_rows = rows * members
    capacity = 2 * rows // devices
    factor = 1.0 / math.sqrt(width)
    passage_emb = jnp.dot(passage_hidden, proj_weight, preferred_element_type=jnp.float32).astype(
        jnp.bfloat16
    )
    query_emb = jnp.dot(query_hidden, proj_weight, preferred_element_type=jnp.float32).astype(
        jnp.bfloat16
    )
    target = cluster * group_rows + place
    owner = target // rows
    slot = target % rows
    order = jnp.arange(rows, dtype=jnp.int32)
    earlier_same = (owner[:, None] == owner[None, :]) & (order[:, None] > order[None, :])
    rank = jnp.sum(earlier_same.astype(jnp.int32), axis=1)
    position = owner * capacity + rank
    tag_width = 128
    tag = jnp.broadcast_to(slot.astype(jnp.bfloat16)[:, None], (rows, tag_width))
    both = jnp.concatenate([passage_emb, passage_hidden, tag], axis=1)
    send_rows = jnp.zeros((devices * capacity, 2 * width + tag_width), jnp.bfloat16)
    send_rows = send_rows.at[:, 2 * width :].set(rows).at[position].set(both)
    got = lax.all_to_all(send_rows, ALL, split_axis=0, concat_axis=0, tiled=True)
    got_rows = got[:, : 2 * width]
    got_slots = got[:, 2 * width].astype(jnp.int32)
    relaid = jnp.zeros((rows, 2 * width), jnp.bfloat16).at[got_slots].set(got_rows, mode="drop")
    group_both = lax.all_gather(relaid, MEMBER, axis=0, tiled=True)
    group_passages = group_both[:, :width]
    group_hidden = group_both[:, width:]
    scores = contract(query_emb, group_passages, 1, 1) * factor
    top = jnp.max(scores, axis=1, keepdims=True)
    lse = top[:, 0] + jnp.log(jnp.sum(jnp.exp(scores - top), axis=1))
    hit = jnp.arange(group_rows, dtype=jnp.int32)[None, :] == positive[:, None]
    loss = lse - jnp.sum(jnp.where(hit, scores, 0.0), axis=1)
    coef = (
        loss_weight[:, None] * (jnp.exp(scores - lse[:, None]) - hit.astype(jnp.float32)) * factor
    ).astype(jnp.bfloat16)
    query_grad = jnp.dot(coef, group_passages, preferred_element_type=jnp.float32).astype(
        jnp.bfloat16
    )
    partial = contract(coef, query_emb, 0, 0)
    local_weight = contract(query_hidden, query_grad, 0, 0) + contract(group_hidden, partial, 0, 0)
    chips = lax.axis_size("chip")
    core = lax.axis_index("core")
    swap = [(0, 1), (1, 0)]
    split = partial.reshape(chips, 2, rows, width)
    kept = jnp.where(core == 0, split[:, 0], split[:, 1])
    given = jnp.where(core == 0, split[:, 1], split[:, 0]).astype(jnp.bfloat16)
    paired = (kept + lax.ppermute(given, "core", swap).astype(jnp.float32)).astype(jnp.bfloat16)
    paired, local_weight = lax.optimization_barrier((paired, local_weight))
    weight_rows = width // members
    weight_split = local_weight.reshape(chips, 2, weight_rows, width)
    weight_kept = jnp.where(core == 0, weight_split[:, 0], weight_split[:, 1])
    weight_given = jnp.where(core == 0, weight_split[:, 1], weight_split[:, 0])
    weight_share = weight_kept + lax.ppermute(weight_given, "core", swap)
    chip = lax.axis_index("chip")
    bit = chips // 2
    while bit >= 1:
        halves = weight_share.reshape(2, -1, weight_rows, width)
        upper = (chip // bit) % 2 == 1
        kept = jnp.where(upper, halves[1], halves[0])
        given = jnp.where(upper, halves[0], halves[1])
        pairs = [(index, index ^ bit) for index in range(chips)]
        weight_share = kept + lax.ppermute(given, "chip", pairs)
        bit //= 2
    weight_share = weight_share.reshape(weight_rows, width)
    step = 1
    while step < groups:
        pairs = [(index, index ^ step) for index in range(groups)]
        weight_share = weight_share + lax.ppermute(weight_share, "group", pairs)
        step *= 2
    grad_weight = lax.all_gather(weight_share, MEMBER, axis=0, tiled=True) / devices
    pieces = lax.all_to_all(
        paired, "chip", split_axis=0, concat_axis=0, tiled=True
    )
    relaid_grad = jnp.sum(pieces.astype(jnp.float32), axis=0).astype(jnp.bfloat16)
    back_rows = relaid_grad[jnp.minimum(got_slots, rows - 1)]
    returned = lax.all_to_all(
        back_rows, ALL, split_axis=0, concat_axis=0, tiled=True
    )
    passage_grad = returned[position]
    grad_passage_hidden = contract(passage_grad, proj_weight, 1, 1).astype(jnp.bfloat16)
    grad_query_hidden = contract(query_grad, proj_weight, 1, 1).astype(jnp.bfloat16)
    return (loss, grad_query_hidden, grad_passage_hidden, grad_weight)


def solution(mesh):
    groups, members = mesh.devices.shape
    mesh = jax.sharding.Mesh(
        mesh.devices.reshape(groups, members // 2, 2), ("group", "chip", "core")
    )
    in_specs = (
        P(("group", "chip", "core"), None),
        P(("group", "chip", "core"), None),
        P(),
        P(("group", "chip", "core")),
        P(("group", "chip", "core")),
        P(("group", "chip", "core")),
        P(("group", "chip", "core")),
    )
    out_specs = (
        P(("group", "chip", "core")),
        P(("group", "chip", "core"), None),
        P(("group", "chip", "core"), None),
        P(),
    )
    return jax.shard_map(body, mesh=mesh, in_specs=in_specs, out_specs=out_specs, check_vma=False)
```

```python
import math

import jax
import jax.numpy as jnp
from jax import lax
from jax.sharding import PartitionSpec as P


MEMBER = ("chip", "core")
ALL = ("group", "chip", "core")


def contract(left, right, left_dim, right_dim):
    return lax.dot_general(
        left, right, (((left_dim,), (right_dim,)), ((), ())), preferred_element_type=jnp.float32
    )


def body(passage_hidden, query_hidden, proj_weight, cluster, place, positive, loss_weight):
    rows, width = passage_hidden.shape
    members = lax.axis_size("chip") * lax.axis_size("core")
    groups = lax.axis_size("group")
    devices = members * groups
    group_rows = rows * members
    capacity = 2 * rows // devices
    factor = 1.0 / math.sqrt(width)
    passage_emb = jnp.dot(passage_hidden, proj_weight, preferred_element_type=jnp.float32).astype(
        jnp.bfloat16
    )
    query_emb = jnp.dot(query_hidden, proj_weight, preferred_element_type=jnp.float32).astype(
        jnp.bfloat16
    )
    target = cluster * group_rows + place
    owner = target // rows
    slot = target % rows
    order = jnp.arange(rows, dtype=jnp.int32)
    earlier_same = (owner[:, None] == owner[None, :]) & (order[:, None] > order[None, :])
    rank = jnp.sum(earlier_same.astype(jnp.int32), axis=1)
    position = owner * capacity + rank
    tag_width = 128
    tag = jnp.broadcast_to(slot.astype(jnp.bfloat16)[:, None], (rows, tag_width))
    both = jnp.concatenate([passage_emb, passage_hidden, tag], axis=1)
    send_rows = jnp.zeros((devices * capacity, 2 * width + tag_width), jnp.bfloat16)
    send_rows = send_rows.at[:, 2 * width :].set(rows).at[position].set(both)
    got = lax.all_to_all(send_rows, ALL, split_axis=0, concat_axis=0, tiled=True)
    got_rows = got[:, : 2 * width]
    got_slots = got[:, 2 * width].astype(jnp.int32)
    relaid = jnp.zeros((rows, 2 * width), jnp.bfloat16).at[got_slots].set(got_rows, mode="drop")
    group_passages = lax.all_gather(relaid[:, :width], MEMBER, axis=0, tiled=True)
    group_hidden = lax.all_gather(relaid[:, width:], MEMBER, axis=0, tiled=True)
    scores = contract(query_emb, group_passages, 1, 1) * factor
    top = jnp.max(scores, axis=1, keepdims=True)
    lse = top[:, 0] + jnp.log(jnp.sum(jnp.exp(scores - top), axis=1))
    hit = jnp.arange(group_rows, dtype=jnp.int32)[None, :] == positive[:, None]
    loss = lse - jnp.sum(jnp.where(hit, scores, 0.0), axis=1)
    coef = (
        loss_weight[:, None] * (jnp.exp(scores - lse[:, None]) - hit.astype(jnp.float32)) * factor
    ).astype(jnp.bfloat16)
    query_grad = jnp.dot(coef, group_passages, preferred_element_type=jnp.float32).astype(
        jnp.bfloat16
    )
    partial = contract(coef, query_emb, 0, 0)
    local_weight = contract(query_hidden, query_grad, 0, 0) + contract(group_hidden, partial, 0, 0)
    weight_rows = width // members
    chips = lax.axis_size("chip")
    core = lax.axis_index("core")
    swap = [(0, 1), (1, 0)]
    weight_split = local_weight.reshape(chips, 2, weight_rows, width)
    weight_kept = jnp.where(core == 0, weight_split[:, 0], weight_split[:, 1])
    weight_given = jnp.where(core == 0, weight_split[:, 1], weight_split[:, 0])
    weight_paired = weight_kept + lax.ppermute(weight_given, "core", swap)
    weight_pieces = lax.all_to_all(weight_paired, "chip", 0, 0, tiled=True)
    weight_share = jnp.sum(weight_pieces, axis=0)
    step = 1
    while step < groups:
        pairs = [(index, index ^ step) for index in range(groups)]
        weight_share = weight_share + lax.ppermute(weight_share, "group", pairs)
        step *= 2
    grad_weight = lax.all_gather(weight_share, MEMBER, axis=0, tiled=True) / devices
    split = partial.reshape(chips, 2, rows, width)
    kept = jnp.where(core == 0, split[:, 0], split[:, 1])
    given = jnp.where(core == 0, split[:, 1], split[:, 0]).astype(jnp.bfloat16)
    paired = kept + lax.ppermute(given, "core", swap).astype(jnp.float32)
    pieces = lax.all_to_all(
        paired.astype(jnp.bfloat16), "chip", split_axis=0, concat_axis=0, tiled=True
    )
    relaid_grad = jnp.sum(pieces.astype(jnp.float32), axis=0).astype(jnp.bfloat16)
    back_rows = relaid_grad[jnp.minimum(got_slots, rows - 1)]
    returned = lax.all_to_all(
        back_rows, ALL, split_axis=0, concat_axis=0, tiled=True
    )
    passage_grad = returned[position]
    grad_passage_hidden = contract(passage_grad, proj_weight, 1, 1).astype(jnp.bfloat16)
    grad_query_hidden = contract(query_grad, proj_weight, 1, 1).astype(jnp.bfloat16)
    return (loss, grad_query_hidden, grad_passage_hidden, grad_weight)


def solution(mesh):
    groups, members = mesh.devices.shape
    mesh = jax.sharding.Mesh(
        mesh.devices.reshape(groups, members // 2, 2), ("group", "chip", "core")
    )
    in_specs = (
        P(("group", "chip", "core"), None),
        P(("group", "chip", "core"), None),
        P(),
        P(("group", "chip", "core")),
        P(("group", "chip", "core")),
        P(("group", "chip", "core")),
        P(("group", "chip", "core")),
    )
    out_specs = (
        P(("group", "chip", "core")),
        P(("group", "chip", "core"), None),
        P(("group", "chip", "core"), None),
        P(),
    )
    return jax.shard_map(body, mesh=mesh, in_specs=in_specs, out_specs=out_specs, check_vma=False)
```

```python
import math

import jax
import jax.numpy as jnp
from jax import lax
from jax.sharding import PartitionSpec as P


MEMBER = ("chip", "core")
ALL = ("group", "chip", "core")


def contract(left, right, left_dim, right_dim):
    return lax.dot_general(
        left, right, (((left_dim,), (right_dim,)), ((), ())), preferred_element_type=jnp.float32
    )


def body(passage_hidden, query_hidden, proj_weight, cluster, place, positive, loss_weight):
    rows, width = passage_hidden.shape
    members = lax.axis_size("chip") * lax.axis_size("core")
    groups = lax.axis_size("group")
    devices = members * groups
    group_rows = rows * members
    capacity = 2 * rows // devices
    factor = 1.0 / math.sqrt(width)
    passage_emb = jnp.dot(passage_hidden, proj_weight, preferred_element_type=jnp.float32).astype(
        jnp.bfloat16
    )
    query_emb = jnp.dot(query_hidden, proj_weight, preferred_element_type=jnp.float32).astype(
        jnp.bfloat16
    )
    target = cluster * group_rows + place
    owner = target // rows
    slot = target % rows
    order = jnp.arange(rows, dtype=jnp.int32)
    earlier_same = (owner[:, None] == owner[None, :]) & (order[:, None] > order[None, :])
    rank = jnp.sum(earlier_same.astype(jnp.int32), axis=1)
    position = owner * capacity + rank
    tag_width = 128
    tag = jnp.broadcast_to(slot.astype(jnp.bfloat16)[:, None], (rows, tag_width))
    both = jnp.concatenate([passage_emb, passage_hidden, tag], axis=1)
    send_rows = jnp.zeros((devices * capacity, 2 * width + tag_width), jnp.bfloat16)
    send_rows = send_rows.at[:, 2 * width :].set(rows).at[position].set(both)
    got = lax.all_to_all(send_rows, ALL, split_axis=0, concat_axis=0, tiled=True)
    got_rows = got[:, : 2 * width]
    got_slots = got[:, 2 * width].astype(jnp.int32)
    relaid = jnp.zeros((rows, 2 * width), jnp.bfloat16).at[got_slots].set(got_rows, mode="drop")
    chips = lax.axis_size("chip")
    chip = lax.axis_index("chip")
    core = lax.axis_index("core")
    swap = [(0, 1), (1, 0)]
    me = chip * 2 + core
    group_both = relaid
    bit = 1
    while bit < chips:
        pairs = [(index, index ^ bit) for index in range(chips)]
        group_both = jnp.concatenate([group_both, lax.ppermute(group_both, "chip", pairs)])
        bit *= 2
    group_both = jnp.concatenate([group_both, lax.ppermute(group_both, "core", swap)])
    relative = positive // rows ^ me
    positive = ((relative % 2) * chips + relative // 2) * rows + positive % rows
    group_passages = group_both[:, :width]
    group_hidden = group_both[:, width:]
    scores = contract(query_emb, group_passages, 1, 1) * factor
    top = jnp.max(scores, axis=1, keepdims=True)
    lse = top[:, 0] + jnp.log(jnp.sum(jnp.exp(scores - top), axis=1))
    hit = jnp.arange(group_rows, dtype=jnp.int32)[None, :] == positive[:, None]
    loss = lse - jnp.sum(jnp.where(hit, scores, 0.0), axis=1)
    coef = (
        loss_weight[:, None] * (jnp.exp(scores - lse[:, None]) - hit.astype(jnp.float32)) * factor
    ).astype(jnp.bfloat16)
    query_grad = jnp.dot(coef, group_passages, preferred_element_type=jnp.float32).astype(
        jnp.bfloat16
    )
    partial = contract(coef, query_emb, 0, 0)
    local_weight = contract(query_hidden, query_grad, 0, 0) + contract(group_hidden, partial, 0, 0)
    weight_rows = width // members
    weight_split = local_weight.reshape(chips, 2, weight_rows, width)
    weight_kept = jnp.where(core == 0, weight_split[:, 0], weight_split[:, 1])
    weight_given = jnp.where(core == 0, weight_split[:, 1], weight_split[:, 0])
    weight_paired = weight_kept + lax.ppermute(weight_given, "core", swap)
    weight_pieces = lax.all_to_all(weight_paired, "chip", 0, 0, tiled=True)
    weight_share = jnp.sum(weight_pieces, axis=0)
    step = 1
    while step < groups:
        pairs = [(index, index ^ step) for index in range(groups)]
        weight_share = weight_share + lax.ppermute(weight_share, "group", pairs)
        step *= 2
    grad_weight = lax.all_gather(weight_share, MEMBER, axis=0, tiled=True) / devices
    kept = partial[: chips * rows].reshape(chips, rows, width)
    given = partial[chips * rows :].reshape(chips, rows, width).astype(jnp.bfloat16)
    paired = kept + lax.ppermute(given, "core", swap).astype(jnp.float32)
    paired = jnp.take(paired, jnp.arange(chips) ^ chip, axis=0)
    pieces = lax.all_to_all(
        paired.astype(jnp.bfloat16), "chip", split_axis=0, concat_axis=0, tiled=True
    )
    relaid_grad = jnp.sum(pieces.astype(jnp.float32), axis=0).astype(jnp.bfloat16)
    back_rows = relaid_grad[jnp.minimum(got_slots, rows - 1)]
    returned = lax.all_to_all(
        back_rows, ALL, split_axis=0, concat_axis=0, tiled=True
    )
    passage_grad = returned[position]
    grad_passage_hidden = contract(passage_grad, proj_weight, 1, 1).astype(jnp.bfloat16)
    grad_query_hidden = contract(query_grad, proj_weight, 1, 1).astype(jnp.bfloat16)
    return (loss, grad_query_hidden, grad_passage_hidden, grad_weight)


def solution(mesh):
    groups, members = mesh.devices.shape
    mesh = jax.sharding.Mesh(
        mesh.devices.reshape(groups, members // 2, 2), ("group", "chip", "core")
    )
    in_specs = (
        P(("group", "chip", "core"), None),
        P(("group", "chip", "core"), None),
        P(),
        P(("group", "chip", "core")),
        P(("group", "chip", "core")),
        P(("group", "chip", "core")),
        P(("group", "chip", "core")),
    )
    out_specs = (
        P(("group", "chip", "core")),
        P(("group", "chip", "core"), None),
        P(("group", "chip", "core"), None),
        P(),
    )
    return jax.shard_map(body, mesh=mesh, in_specs=in_specs, out_specs=out_specs, check_vma=False)
```

```python
import math

import jax
import jax.numpy as jnp
from jax import lax
from jax.sharding import PartitionSpec as P


MEMBER = ("chip", "core")
ALL = ("group", "chip", "core")


def contract(left, right, left_dim, right_dim):
    return lax.dot_general(
        left, right, (((left_dim,), (right_dim,)), ((), ())), preferred_element_type=jnp.float32
    )


def body(passage_hidden, query_hidden, proj_weight, cluster, place, positive, loss_weight):
    rows, width = passage_hidden.shape
    members = lax.axis_size("chip") * lax.axis_size("core")
    groups = lax.axis_size("group")
    devices = members * groups
    group_rows = rows * members
    capacity = 2 * rows // devices
    factor = 1.0 / math.sqrt(width)
    passage_emb = jnp.dot(passage_hidden, proj_weight, preferred_element_type=jnp.float32).astype(
        jnp.bfloat16
    )
    query_emb = jnp.dot(query_hidden, proj_weight, preferred_element_type=jnp.float32).astype(
        jnp.bfloat16
    )
    target = cluster * group_rows + place
    owner = target // rows
    slot = target % rows
    order = jnp.arange(rows, dtype=jnp.int32)
    earlier_same = (owner[:, None] == owner[None, :]) & (order[:, None] > order[None, :])
    rank = jnp.sum(earlier_same.astype(jnp.int32), axis=1)
    position = owner * capacity + rank
    tag_width = 128
    tag = jnp.broadcast_to(slot.astype(jnp.bfloat16)[:, None], (rows, tag_width))
    both = jnp.concatenate([passage_emb, passage_hidden, tag], axis=1)
    send_rows = jnp.zeros((devices * capacity, 2 * width + tag_width), jnp.bfloat16)
    send_rows = send_rows.at[:, 2 * width :].set(rows).at[position].set(both)
    got = lax.all_to_all(send_rows, ALL, split_axis=0, concat_axis=0, tiled=True)
    got_rows = got[:, : 2 * width]
    got_slots = got[:, 2 * width].astype(jnp.int32)
    relaid = jnp.zeros((rows, 2 * width), jnp.bfloat16).at[got_slots].set(got_rows, mode="drop")
    group_both = lax.all_gather(relaid, MEMBER, axis=0, tiled=True)
    group_passages = group_both[:, :width]
    group_hidden = group_both[:, width:]
    scores = contract(query_emb, group_passages, 1, 1) * factor
    top = jnp.max(scores, axis=1, keepdims=True)
    lse = top[:, 0] + jnp.log(jnp.sum(jnp.exp(scores - top), axis=1))
    hit = jnp.arange(group_rows, dtype=jnp.int32)[None, :] == positive[:, None]
    loss = lse - jnp.sum(jnp.where(hit, scores, 0.0), axis=1)
    coef = (
        loss_weight[:, None] * (jnp.exp(scores - lse[:, None]) - hit.astype(jnp.float32)) * factor
    ).astype(jnp.bfloat16)
    query_grad = jnp.dot(coef, group_passages, preferred_element_type=jnp.float32).astype(
        jnp.bfloat16
    )
    chips = members // 2
    core = lax.axis_index("core")
    coef_split = coef.reshape(-1, chips, 2, rows)
    hidden_split = group_hidden.reshape(chips, 2, rows, width)
    own_coef = lax.dynamic_index_in_dim(coef_split, core, axis=2, keepdims=False)
    other_coef = lax.dynamic_index_in_dim(coef_split, 1 - core, axis=2, keepdims=False)
    own_hidden = lax.dynamic_index_in_dim(hidden_split, core, axis=1, keepdims=False)
    other_hidden = lax.dynamic_index_in_dim(hidden_split, 1 - core, axis=1, keepdims=False)
    kept = lax.dot_general(
        own_coef, query_emb, (((0,), (0,)), ((), ())), preferred_element_type=jnp.float32
    )
    other = lax.dot_general(
        other_coef, query_emb, (((0,), (0,)), ((), ())), preferred_element_type=jnp.float32
    )
    passage_term = lax.dot_general(
        own_hidden, kept, (((0, 1), (0, 1)), ((), ())), preferred_element_type=jnp.float32
    ) + lax.dot_general(
        other_hidden, other, (((0, 1), (0, 1)), ((), ())), preferred_element_type=jnp.float32
    )
    local_weight = contract(query_hidden, query_grad, 0, 0) + passage_term
    weight_rows = width // members
    swap = [(0, 1), (1, 0)]
    weight_split = local_weight.reshape(chips, 2, weight_rows, width)
    weight_kept = jnp.where(core == 0, weight_split[:, 0], weight_split[:, 1])
    weight_given = jnp.where(core == 0, weight_split[:, 1], weight_split[:, 0])
    weight_paired = weight_kept + lax.ppermute(weight_given, "core", swap)
    weight_pieces = lax.all_to_all(weight_paired, "chip", 0, 0, tiled=True)
    weight_share = jnp.sum(weight_pieces, axis=0)
    step = 1
    while step < groups:
        pairs = [(index, index ^ step) for index in range(groups)]
        weight_share = weight_share + lax.ppermute(weight_share, "group", pairs)
        step *= 2
    grad_weight = lax.all_gather(weight_share / devices, MEMBER, axis=0, tiled=True)
    given = other.astype(jnp.bfloat16)
    paired = kept + lax.ppermute(given, "core", swap).astype(jnp.float32)
    pieces = lax.all_to_all(
        paired.astype(jnp.bfloat16), "chip", split_axis=0, concat_axis=0, tiled=True
    )
    relaid_grad = jnp.sum(pieces.astype(jnp.float32), axis=0).astype(jnp.bfloat16)
    back_rows = relaid_grad[jnp.minimum(got_slots, rows - 1)]
    returned = lax.all_to_all(
        back_rows, ALL, split_axis=0, concat_axis=0, tiled=True
    )
    passage_grad = returned[position]
    grad_passage_hidden = contract(passage_grad, proj_weight, 1, 1).astype(jnp.bfloat16)
    grad_query_hidden = contract(query_grad, proj_weight, 1, 1).astype(jnp.bfloat16)
    return (loss, grad_query_hidden, grad_passage_hidden, grad_weight)


def solution(mesh):
    groups, members = mesh.devices.shape
    mesh = jax.sharding.Mesh(
        mesh.devices.reshape(groups, members // 2, 2), ("group", "chip", "core")
    )
    in_specs = (
        P(("group", "chip", "core"), None),
        P(("group", "chip", "core"), None),
        P(),
        P(("group", "chip", "core")),
        P(("group", "chip", "core")),
        P(("group", "chip", "core")),
        P(("group", "chip", "core")),
    )
    out_specs = (
        P(("group", "chip", "core")),
        P(("group", "chip", "core"), None),
        P(("group", "chip", "core"), None),
        P(),
    )
    return jax.shard_map(body, mesh=mesh, in_specs=in_specs, out_specs=out_specs, check_vma=False)
```

```python
import math

import jax
import jax.numpy as jnp
from jax import lax
from jax.sharding import PartitionSpec as P


MEMBER = ("chip", "core")
ALL = ("group", "chip", "core")


def contract(left, right, left_dim, right_dim):
    return lax.dot_general(
        left, right, (((left_dim,), (right_dim,)), ((), ())), preferred_element_type=jnp.float32
    )


def body(passage_hidden, query_hidden, proj_weight, cluster, place, positive, loss_weight):
    rows, width = passage_hidden.shape
    members = lax.axis_size("chip") * lax.axis_size("core")
    groups = lax.axis_size("group")
    devices = members * groups
    group_rows = rows * members
    capacity = 2 * rows // devices
    factor = 1.0 / math.sqrt(width)
    passage_emb = jnp.dot(passage_hidden, proj_weight, preferred_element_type=jnp.float32).astype(
        jnp.bfloat16
    )
    query_emb = jnp.dot(query_hidden, proj_weight, preferred_element_type=jnp.float32).astype(
        jnp.bfloat16
    )
    target = cluster * group_rows + place
    owner = target // rows
    slot = target % rows
    order = jnp.arange(rows, dtype=jnp.int32)
    earlier_same = (owner[:, None] == owner[None, :]) & (order[:, None] > order[None, :])
    rank = jnp.sum(earlier_same.astype(jnp.int32), axis=1)
    position = owner * capacity + rank
    tag_width = 128
    tag = jnp.broadcast_to(slot.astype(jnp.bfloat16)[:, None], (rows, tag_width))
    both = jnp.concatenate([passage_emb, passage_hidden, tag], axis=1)
    send_rows = jnp.zeros((devices * capacity, 2 * width + tag_width), jnp.bfloat16)
    send_rows = send_rows.at[:, 2 * width :].set(rows).at[position].set(both)
    got = lax.all_to_all(send_rows, ALL, split_axis=0, concat_axis=0, tiled=True)
    got_rows = got[:, : 2 * width]
    got_slots = got[:, 2 * width].astype(jnp.int32)
    relaid = jnp.zeros((rows, 2 * width), jnp.bfloat16).at[got_slots].set(got_rows, mode="drop")
    group_both = lax.all_gather(relaid, MEMBER, axis=0, tiled=True)
    group_passages = group_both[:, :width]
    group_hidden = group_both[:, width:]
    scores = contract(query_emb, group_passages, 1, 1) * factor
    top = jnp.max(scores, axis=1, keepdims=True)
    lse = top[:, 0] + jnp.log(jnp.sum(jnp.exp(scores - top), axis=1))
    hit = jnp.arange(group_rows, dtype=jnp.int32)[None, :] == positive[:, None]
    loss = lse - jnp.sum(jnp.where(hit, scores, 0.0), axis=1)
    coef = (
        loss_weight[:, None] * (jnp.exp(scores - lse[:, None]) - hit.astype(jnp.float32)) * factor
    ).astype(jnp.bfloat16)
    query_grad = jnp.dot(coef, group_passages, preferred_element_type=jnp.float32).astype(
        jnp.bfloat16
    )
    partial = contract(coef, query_emb, 0, 0)
    local_weight = contract(query_hidden, query_grad, 0, 0) + contract(group_hidden, partial, 0, 0)
    weight_rows = width // members
    chips = lax.axis_size("chip")
    core = lax.axis_index("core")
    swap = [(0, 1), (1, 0)]
    weight_split = local_weight.reshape(chips, 2, weight_rows, width)
    weight_kept = jnp.where(core == 0, weight_split[:, 0], weight_split[:, 1])
    weight_given = jnp.where(core == 0, weight_split[:, 1], weight_split[:, 0])
    weight_paired = weight_kept + lax.ppermute(weight_given, "core", swap)
    weight_pieces = lax.all_to_all(weight_paired, "chip", 0, 0, tiled=True)
    weight_share = jnp.sum(weight_pieces, axis=0)
    step = 1
    while step < groups:
        pairs = [(index, index ^ step) for index in range(groups)]
        weight_share = weight_share + lax.ppermute(weight_share, "group", pairs)
        step *= 2
    grad_weight = lax.all_gather(weight_share / devices, MEMBER, axis=0, tiled=True)
    split = partial.reshape(chips, 2, rows, width)
    kept = jnp.where(core == 0, split[:, 0], split[:, 1])
    given = jnp.where(core == 0, split[:, 1], split[:, 0]).astype(jnp.bfloat16)
    paired = kept + lax.ppermute(given, "core", swap).astype(jnp.float32)
    pieces = lax.all_to_all(
        paired.astype(jnp.bfloat16), "chip", split_axis=0, concat_axis=0, tiled=True
    )
    relaid_grad = jnp.sum(pieces.astype(jnp.float32), axis=0).astype(jnp.bfloat16)
    back_rows = relaid_grad[jnp.minimum(got_slots, rows - 1)]
    returned = lax.all_to_all(
        back_rows, ALL, split_axis=0, concat_axis=0, tiled=True
    )
    passage_grad = returned[position]
    grad_passage_hidden = contract(passage_grad, proj_weight, 1, 1).astype(jnp.bfloat16)
    grad_query_hidden = contract(query_grad, proj_weight, 1, 1).astype(jnp.bfloat16)
    return (loss, grad_query_hidden, grad_passage_hidden, grad_weight)


def solution(mesh):
    groups, members = mesh.devices.shape
    mesh = jax.sharding.Mesh(
        mesh.devices.reshape(groups, members // 2, 2), ("group", "chip", "core")
    )
    in_specs = (
        P(("group", "chip", "core"), None),
        P(("group", "chip", "core"), None),
        P(),
        P(("group", "chip", "core")),
        P(("group", "chip", "core")),
        P(("group", "chip", "core")),
        P(("group", "chip", "core")),
    )
    out_specs = (
        P(("group", "chip", "core")),
        P(("group", "chip", "core"), None),
        P(("group", "chip", "core"), None),
        P(),
    )
    return jax.shard_map(body, mesh=mesh, in_specs=in_specs, out_specs=out_specs, check_vma=False)
```

```python
import math

import jax
import jax.numpy as jnp
from jax import lax
from jax.sharding import PartitionSpec as P


MEMBER = ("chip", "core")
ALL = ("group", "chip", "core")


def contract(left, right, left_dim, right_dim):
    return lax.dot_general(
        left, right, (((left_dim,), (right_dim,)), ((), ())), preferred_element_type=jnp.float32
    )


def body(passage_hidden, query_hidden, proj_weight, cluster, place, positive, loss_weight):
    rows, width = passage_hidden.shape
    members = lax.axis_size("chip") * lax.axis_size("core")
    groups = lax.axis_size("group")
    devices = members * groups
    group_rows = rows * members
    capacity = 2 * rows // devices
    factor = 1.0 / math.sqrt(width)
    passage_emb = jnp.dot(passage_hidden, proj_weight, preferred_element_type=jnp.float32).astype(
        jnp.bfloat16
    )
    query_emb = jnp.dot(query_hidden, proj_weight, preferred_element_type=jnp.float32).astype(
        jnp.bfloat16
    )
    target = cluster * group_rows + place
    owner = target // rows
    slot = target % rows
    order = jnp.arange(rows, dtype=jnp.int32)
    earlier_same = (owner[:, None] == owner[None, :]) & (order[:, None] > order[None, :])
    rank = jnp.sum(earlier_same.astype(jnp.int32), axis=1)
    position = owner * capacity + rank
    tag_width = 128
    tag = jnp.broadcast_to(slot.astype(jnp.bfloat16)[:, None], (rows, tag_width))
    both = jnp.concatenate([passage_emb, passage_hidden, tag], axis=1)
    send_rows = jnp.zeros((devices * capacity, 2 * width + tag_width), jnp.bfloat16)
    send_rows = send_rows.at[:, 2 * width :].set(rows).at[position].set(both)
    got = lax.all_to_all(send_rows, ALL, split_axis=0, concat_axis=0, tiled=True)
    got_rows = got[:, : 2 * width]
    got_slots = got[:, 2 * width].astype(jnp.int32)
    relaid = jnp.zeros((rows, 2 * width), jnp.bfloat16).at[got_slots].set(got_rows, mode="drop")
    group_both = lax.all_gather(relaid, ("core", "chip"), axis=0, tiled=True)
    half = group_rows // 2
    positive_member = positive // rows
    positive = positive_member % 2 * half + positive_member // 2 * rows + positive % rows
    group_passages = group_both[:, :width]
    group_hidden = group_both[:, width:]
    scores = contract(query_emb, group_passages, 1, 1) * factor
    top = jnp.max(scores, axis=1, keepdims=True)
    lse = top[:, 0] + jnp.log(jnp.sum(jnp.exp(scores - top), axis=1))
    hit = jnp.arange(group_rows, dtype=jnp.int32)[None, :] == positive[:, None]
    loss = lse - jnp.sum(jnp.where(hit, scores, 0.0), axis=1)
    coef = (
        loss_weight[:, None] * (jnp.exp(scores - lse[:, None]) - hit.astype(jnp.float32)) * factor
    ).astype(jnp.bfloat16)
    query_grad = jnp.dot(coef, group_passages, preferred_element_type=jnp.float32).astype(
        jnp.bfloat16
    )
    core = lax.axis_index("core")
    own_coef = lax.dynamic_slice_in_dim(coef, core * half, half, axis=1)
    other_coef = lax.dynamic_slice_in_dim(coef, (1 - core) * half, half, axis=1)
    own_partial = contract(own_coef, query_emb, 0, 0)
    other_partial = contract(other_coef, query_emb, 0, 0)
    own_hidden = lax.dynamic_slice_in_dim(group_hidden, core * half, half)
    other_hidden = lax.dynamic_slice_in_dim(group_hidden, (1 - core) * half, half)
    local_weight = (
        contract(query_hidden, query_grad, 0, 0)
        + contract(own_hidden, own_partial, 0, 0)
        + contract(other_hidden, other_partial, 0, 0)
    )
    weight_rows = width // members
    chips = lax.axis_size("chip")
    core = lax.axis_index("core")
    swap = [(0, 1), (1, 0)]
    weight_split = local_weight.reshape(chips, 2, weight_rows, width)
    weight_kept = jnp.where(core == 0, weight_split[:, 0], weight_split[:, 1])
    weight_given = jnp.where(core == 0, weight_split[:, 1], weight_split[:, 0])
    weight_paired = weight_kept + lax.ppermute(weight_given, "core", swap)
    weight_pieces = lax.all_to_all(weight_paired, "chip", 0, 0, tiled=True)
    weight_share = jnp.sum(weight_pieces, axis=0)
    step = 1
    while step < groups:
        pairs = [(index, index ^ step) for index in range(groups)]
        weight_share = weight_share + lax.ppermute(weight_share, "group", pairs)
        step *= 2
    grad_weight = lax.all_gather(weight_share / devices, MEMBER, axis=0, tiled=True)
    kept = own_partial.reshape(chips, rows, width)
    given = other_partial.reshape(chips, rows, width).astype(jnp.bfloat16)
    paired = kept + lax.ppermute(given, "core", swap).astype(jnp.float32)
    pieces = lax.all_to_all(
        paired.astype(jnp.bfloat16), "chip", split_axis=0, concat_axis=0, tiled=True
    )
    relaid_grad = jnp.sum(pieces.astype(jnp.float32), axis=0).astype(jnp.bfloat16)
    back_rows = relaid_grad[jnp.minimum(got_slots, rows - 1)]
    returned = lax.all_to_all(
        back_rows, ALL, split_axis=0, concat_axis=0, tiled=True
    )
    passage_grad = returned[position]
    grad_passage_hidden = contract(passage_grad, proj_weight, 1, 1).astype(jnp.bfloat16)
    grad_query_hidden = contract(query_grad, proj_weight, 1, 1).astype(jnp.bfloat16)
    return (loss, grad_query_hidden, grad_passage_hidden, grad_weight)


def solution(mesh):
    groups, members = mesh.devices.shape
    mesh = jax.sharding.Mesh(
        mesh.devices.reshape(groups, members // 2, 2), ("group", "chip", "core")
    )
    in_specs = (
        P(("group", "chip", "core"), None),
        P(("group", "chip", "core"), None),
        P(),
        P(("group", "chip", "core")),
        P(("group", "chip", "core")),
        P(("group", "chip", "core")),
        P(("group", "chip", "core")),
    )
    out_specs = (
        P(("group", "chip", "core")),
        P(("group", "chip", "core"), None),
        P(("group", "chip", "core"), None),
        P(),
    )
    return jax.shard_map(body, mesh=mesh, in_specs=in_specs, out_specs=out_specs, check_vma=False)
```

```python
import math

import jax
import jax.numpy as jnp
from jax import lax
from jax.sharding import PartitionSpec as P


ALL = ("group", "chip", "core")


def contract(left, right, left_dim, right_dim):
    return lax.dot_general(
        left, right, (((left_dim,), (right_dim,)), ((), ())), preferred_element_type=jnp.float32
    )


def body(passage_hidden, query_hidden, proj_weight, cluster, place, positive, loss_weight):
    rows, width = passage_hidden.shape
    members = lax.axis_size("chip") * lax.axis_size("core")
    groups = lax.axis_size("group")
    devices = members * groups
    group_rows = rows * members
    capacity = 2 * rows // devices
    factor = 1.0 / math.sqrt(width)
    passage_emb = jnp.dot(passage_hidden, proj_weight, preferred_element_type=jnp.float32).astype(
        jnp.bfloat16
    )
    query_emb = jnp.dot(query_hidden, proj_weight, preferred_element_type=jnp.float32).astype(
        jnp.bfloat16
    )
    target = cluster * group_rows + place
    owner = target // rows
    slot = target % rows
    order = jnp.arange(rows, dtype=jnp.int32)
    earlier_same = (owner[:, None] == owner[None, :]) & (order[:, None] > order[None, :])
    rank = jnp.sum(earlier_same.astype(jnp.int32), axis=1)
    position = owner * capacity + rank
    tag_width = 128
    tag = jnp.broadcast_to(slot.astype(jnp.bfloat16)[:, None], (rows, tag_width))
    both = jnp.concatenate([passage_emb, passage_hidden, tag], axis=1)
    send_rows = jnp.zeros((devices * capacity, 2 * width + tag_width), jnp.bfloat16)
    send_rows = send_rows.at[:, 2 * width :].set(rows).at[position].set(both)
    got = lax.all_to_all(send_rows, ALL, split_axis=0, concat_axis=0, tiled=True)
    got_rows = got[:, : 2 * width]
    got_slots = got[:, 2 * width].astype(jnp.int32)
    relaid = jnp.zeros((rows, 2 * width), jnp.bfloat16).at[got_slots].set(got_rows, mode="drop")
    group_both = lax.all_gather(relaid, ("core", "chip"), axis=0, tiled=True)
    half = group_rows // 2
    positive_member = positive // rows
    positive = positive_member % 2 * half + positive_member // 2 * rows + positive % rows
    group_passages = group_both[:, :width]
    group_hidden = group_both[:, width:]
    scores = contract(query_emb, group_passages, 1, 1) * factor
    top = jnp.max(scores, axis=1, keepdims=True)
    lse = top[:, 0] + jnp.log(jnp.sum(jnp.exp(scores - top), axis=1))
    hit = jnp.arange(group_rows, dtype=jnp.int32)[None, :] == positive[:, None]
    loss = lse - jnp.sum(jnp.where(hit, scores, 0.0), axis=1)
    coef = (
        loss_weight[:, None] * (jnp.exp(scores - lse[:, None]) - hit.astype(jnp.float32)) * factor
    ).astype(jnp.bfloat16)
    query_grad = jnp.dot(coef, group_passages, preferred_element_type=jnp.float32).astype(
        jnp.bfloat16
    )
    partial = contract(coef, query_emb, 0, 0)
    local_weight = contract(query_hidden, query_grad, 0, 0) + contract(group_hidden, partial, 0, 0)
    chips = lax.axis_size("chip")
    core = lax.axis_index("core")
    swap = [(0, 1), (1, 0)]
    weight_split = local_weight.reshape(2, groups * chips, width // devices, width)
    weight_kept = jnp.where(core == 0, weight_split[0], weight_split[1])
    weight_given = jnp.where(core == 0, weight_split[1], weight_split[0])
    weight_paired = weight_kept + lax.ppermute(weight_given, "core", swap)
    weight_pieces = lax.all_to_all(weight_paired, ("group", "chip"), 0, 0, tiled=True)
    weight_share = jnp.sum(weight_pieces, axis=0)
    grad_weight = lax.all_gather(
        weight_share / devices, ("core", "group", "chip"), axis=0, tiled=True
    )
    kept = lax.dynamic_slice_in_dim(partial, core * half, half).reshape(chips, rows, width)
    given = lax.dynamic_slice_in_dim(partial, (1 - core) * half, half)
    given = given.reshape(chips, rows, width).astype(jnp.bfloat16)
    paired = kept + lax.ppermute(given, "core", swap).astype(jnp.float32)
    pieces = lax.all_to_all(
        paired.astype(jnp.bfloat16), "chip", split_axis=0, concat_axis=0, tiled=True
    )
    relaid_grad = jnp.sum(pieces.astype(jnp.float32), axis=0).astype(jnp.bfloat16)
    back_rows = relaid_grad[jnp.minimum(got_slots, rows - 1)]
    returned = lax.all_to_all(
        back_rows, ALL, split_axis=0, concat_axis=0, tiled=True
    )
    passage_grad = returned[position]
    grad_passage_hidden = contract(passage_grad, proj_weight, 1, 1).astype(jnp.bfloat16)
    grad_query_hidden = contract(query_grad, proj_weight, 1, 1).astype(jnp.bfloat16)
    return (loss, grad_query_hidden, grad_passage_hidden, grad_weight)


def solution(mesh):
    groups, members = mesh.devices.shape
    mesh = jax.sharding.Mesh(
        mesh.devices.reshape(groups, members // 2, 2), ("group", "chip", "core")
    )
    in_specs = (
        P(("group", "chip", "core"), None),
        P(("group", "chip", "core"), None),
        P(),
        P(("group", "chip", "core")),
        P(("group", "chip", "core")),
        P(("group", "chip", "core")),
        P(("group", "chip", "core")),
    )
    out_specs = (
        P(("group", "chip", "core")),
        P(("group", "chip", "core"), None),
        P(("group", "chip", "core"), None),
        P(),
    )
    return jax.shard_map(body, mesh=mesh, in_specs=in_specs, out_specs=out_specs, check_vma=False)
```

```python
import math

import jax
import jax.numpy as jnp
from jax import lax
from jax.sharding import PartitionSpec as P


MEMBER = ("chip", "core")
ALL = ("group", "chip", "core")


def contract(left, right, left_dim, right_dim):
    return lax.dot_general(
        left, right, (((left_dim,), (right_dim,)), ((), ())), preferred_element_type=jnp.float32
    )


def body(passage_hidden, query_hidden, proj_weight, cluster, place, positive, loss_weight):
    rows, width = passage_hidden.shape
    members = lax.axis_size("chip") * lax.axis_size("core")
    groups = lax.axis_size("group")
    devices = members * groups
    group_rows = rows * members
    capacity = 2 * rows // devices
    factor = 1.0 / math.sqrt(width)
    passage_emb = jnp.dot(passage_hidden, proj_weight, preferred_element_type=jnp.float32).astype(
        jnp.bfloat16
    )
    query_emb = jnp.dot(query_hidden, proj_weight, preferred_element_type=jnp.float32).astype(
        jnp.bfloat16
    )
    target = cluster * group_rows + place
    owner = target // rows
    slot = target % rows
    order = jnp.arange(rows, dtype=jnp.int32)
    earlier_same = (owner[:, None] == owner[None, :]) & (order[:, None] > order[None, :])
    rank = jnp.sum(earlier_same.astype(jnp.int32), axis=1)
    position = owner * capacity + rank
    tag_width = 128
    tag = jnp.broadcast_to(slot.astype(jnp.bfloat16)[:, None], (rows, tag_width))
    both = jnp.concatenate([passage_emb, passage_hidden, tag], axis=1)
    send_rows = jnp.zeros((devices * capacity, 2 * width + tag_width), jnp.bfloat16)
    send_rows = send_rows.at[:, 2 * width :].set(rows).at[position].set(both)
    got = lax.all_to_all(send_rows, ALL, split_axis=0, concat_axis=0, tiled=True)
    got_rows = got[:, : 2 * width]
    got_slots = got[:, 2 * width].astype(jnp.int32)
    relaid = jnp.zeros((rows, 2 * width), jnp.bfloat16).at[got_slots].set(got_rows, mode="drop")
    group_both = lax.all_gather(relaid, ("core", "chip"), axis=0, tiled=True)
    half = group_rows // 2
    positive_member = positive // rows
    positive = positive_member % 2 * half + positive_member // 2 * rows + positive % rows
    group_passages = group_both[:, :width]
    group_hidden = group_both[:, width:]
    scores = contract(query_emb, group_passages, 1, 1) * factor
    top = jnp.max(scores, axis=1, keepdims=True)
    lse = top[:, 0] + jnp.log(jnp.sum(jnp.exp(scores - top), axis=1))
    hit = jnp.arange(group_rows, dtype=jnp.int32)[None, :] == positive[:, None]
    loss = lse - jnp.sum(jnp.where(hit, scores, 0.0), axis=1)
    coef = (
        loss_weight[:, None] * (jnp.exp(scores - lse[:, None]) - hit.astype(jnp.float32)) * factor
    ).astype(jnp.bfloat16)
    query_grad = jnp.dot(coef, group_passages, preferred_element_type=jnp.float32).astype(
        jnp.bfloat16
    )
    partial = contract(coef, query_emb, 0, 0)
    local_weight = contract(query_hidden, query_grad, 0, 0) + contract(group_hidden, partial, 0, 0)
    weight_rows = width // members
    chips = lax.axis_size("chip")
    core = lax.axis_index("core")
    swap = [(0, 1), (1, 0)]
    weight_split = local_weight.reshape(chips, 2, weight_rows, width)
    weight_kept = jnp.where(core == 0, weight_split[:, 0], weight_split[:, 1])
    weight_given = jnp.where(core == 0, weight_split[:, 1], weight_split[:, 0])
    weight_paired = weight_kept + lax.ppermute(weight_given, "core", swap)
    weight_pieces = lax.all_to_all(weight_paired, "chip", 0, 0, tiled=True)
    weight_share = jnp.sum(weight_pieces, axis=0)
    step = 1
    while step < groups:
        pairs = [(index, index ^ step) for index in range(groups)]
        weight_share = weight_share + lax.ppermute(weight_share, "group", pairs)
        step *= 2
    grad_weight = lax.all_gather(weight_share / devices, MEMBER, axis=0, tiled=True)
    kept = jnp.where(core == 0, partial[:half], partial[half:]).reshape(chips, rows, width)
    given = lax.dynamic_slice_in_dim(partial, (1 - core) * half, half)
    given = given.reshape(chips, rows, width).astype(jnp.bfloat16)
    paired = kept + lax.ppermute(given, "core", swap).astype(jnp.float32)
    pieces = lax.all_to_all(
        paired.astype(jnp.bfloat16), "chip", split_axis=0, concat_axis=0, tiled=True
    )
    relaid_grad = jnp.sum(pieces.astype(jnp.float32), axis=0).astype(jnp.bfloat16)
    back_rows = relaid_grad[jnp.minimum(got_slots, rows - 1)]
    returned = lax.all_to_all(
        back_rows, ALL, split_axis=0, concat_axis=0, tiled=True
    )
    passage_grad = returned[position]
    grad_passage_hidden = contract(passage_grad, proj_weight, 1, 1).astype(jnp.bfloat16)
    grad_query_hidden = contract(query_grad, proj_weight, 1, 1).astype(jnp.bfloat16)
    return (loss, grad_query_hidden, grad_passage_hidden, grad_weight)


def solution(mesh):
    groups, members = mesh.devices.shape
    mesh = jax.sharding.Mesh(
        mesh.devices.reshape(groups, members // 2, 2), ("group", "chip", "core")
    )
    in_specs = (
        P(("group", "chip", "core"), None),
        P(("group", "chip", "core"), None),
        P(),
        P(("group", "chip", "core")),
        P(("group", "chip", "core")),
        P(("group", "chip", "core")),
        P(("group", "chip", "core")),
    )
    out_specs = (
        P(("group", "chip", "core")),
        P(("group", "chip", "core"), None),
        P(("group", "chip", "core"), None),
        P(),
    )
    return jax.shard_map(body, mesh=mesh, in_specs=in_specs, out_specs=out_specs, check_vma=False)
```

```python
import math

import jax
import jax.numpy as jnp
from jax import lax
from jax.sharding import PartitionSpec as P


ALL = ("group", "chip", "core")


def contract(left, right, left_dim, right_dim):
    return lax.dot_general(
        left, right, (((left_dim,), (right_dim,)), ((), ())), preferred_element_type=jnp.float32
    )


def body(passage_hidden, query_hidden, proj_weight, cluster, place, positive, loss_weight):
    rows, width = passage_hidden.shape
    members = lax.axis_size("chip") * lax.axis_size("core")
    groups = lax.axis_size("group")
    devices = members * groups
    group_rows = rows * members
    capacity = 2 * rows // devices
    factor = 1.0 / math.sqrt(width)
    passage_emb = jnp.dot(passage_hidden, proj_weight, preferred_element_type=jnp.float32).astype(
        jnp.bfloat16
    )
    query_emb = jnp.dot(query_hidden, proj_weight, preferred_element_type=jnp.float32).astype(
        jnp.bfloat16
    )
    target = cluster * group_rows + place
    owner = target // rows
    slot = target % rows
    order = jnp.arange(rows, dtype=jnp.int32)
    earlier_same = (owner[:, None] == owner[None, :]) & (order[:, None] > order[None, :])
    rank = jnp.sum(earlier_same.astype(jnp.int32), axis=1)
    position = owner * capacity + rank
    tag_width = 128
    tag = jnp.broadcast_to(slot.astype(jnp.bfloat16)[:, None], (rows, tag_width))
    both = jnp.concatenate([passage_emb, passage_hidden, tag], axis=1)
    send_rows = jnp.zeros((devices * capacity, 2 * width + tag_width), jnp.bfloat16)
    send_rows = send_rows.at[:, 2 * width :].set(rows).at[position].set(both)
    got = lax.all_to_all(send_rows, ALL, split_axis=0, concat_axis=0, tiled=True)
    got_rows = got[:, : 2 * width]
    got_slots = got[:, 2 * width].astype(jnp.int32)
    relaid = jnp.zeros((rows, 2 * width), jnp.bfloat16).at[got_slots].set(got_rows, mode="drop")
    group_both = lax.all_gather(relaid, ("core", "chip"), axis=0, tiled=True)
    half = group_rows // 2
    positive_member = positive // rows
    positive = positive_member % 2 * half + positive_member // 2 * rows + positive % rows
    group_passages = group_both[:, :width]
    group_hidden = group_both[:, width:]
    scores = contract(query_emb, group_passages, 1, 1) * factor
    top = jnp.max(scores, axis=1, keepdims=True)
    lse = top[:, 0] + jnp.log(jnp.sum(jnp.exp(scores - top), axis=1))
    hit = jnp.arange(group_rows, dtype=jnp.int32)[None, :] == positive[:, None]
    loss = lse - jnp.sum(jnp.where(hit, scores, 0.0), axis=1)
    coef = (
        loss_weight[:, None] * (jnp.exp(scores - lse[:, None]) - hit.astype(jnp.float32)) * factor
    ).astype(jnp.bfloat16)
    query_grad = jnp.dot(coef, group_passages, preferred_element_type=jnp.float32).astype(
        jnp.bfloat16
    )
    partial = contract(coef, query_emb, 0, 0)
    local_weight = contract(query_hidden, query_grad, 0, 0) + contract(group_hidden, partial, 0, 0)
    weight_rows = width // members
    chips = lax.axis_size("chip")
    core = lax.axis_index("core")
    swap = [(0, 1), (1, 0)]
    weight_split = local_weight.reshape(2, chips, weight_rows, width)
    weight_kept = jnp.where(core == 0, weight_split[0], weight_split[1])
    weight_given = jnp.where(core == 0, weight_split[1], weight_split[0])
    weight_paired = weight_kept + lax.ppermute(weight_given, "core", swap)
    weight_pieces = lax.all_to_all(weight_paired, "chip", 0, 0, tiled=True)
    weight_share = jnp.sum(weight_pieces, axis=0)
    step = 1
    while step < groups:
        pairs = [(index, index ^ step) for index in range(groups)]
        weight_share = weight_share + lax.ppermute(weight_share, "group", pairs)
        step *= 2
    grad_weight = lax.all_gather(weight_share / devices, ("core", "chip"), axis=0, tiled=True)
    kept = lax.dynamic_slice_in_dim(partial, core * half, half).reshape(chips, rows, width)
    given = lax.dynamic_slice_in_dim(partial, (1 - core) * half, half)
    given = given.reshape(chips, rows, width).astype(jnp.bfloat16)
    paired = kept + lax.ppermute(given, "core", swap).astype(jnp.float32)
    pieces = lax.all_to_all(
        paired.astype(jnp.bfloat16), "chip", split_axis=0, concat_axis=0, tiled=True
    )
    relaid_grad = jnp.sum(pieces.astype(jnp.float32), axis=0).astype(jnp.bfloat16)
    back_rows = relaid_grad[jnp.minimum(got_slots, rows - 1)]
    returned = lax.all_to_all(
        back_rows, ALL, split_axis=0, concat_axis=0, tiled=True
    )
    passage_grad = returned[position]
    grad_passage_hidden = contract(passage_grad, proj_weight, 1, 1).astype(jnp.bfloat16)
    grad_query_hidden = contract(query_grad, proj_weight, 1, 1).astype(jnp.bfloat16)
    return (loss, grad_query_hidden, grad_passage_hidden, grad_weight)


def solution(mesh):
    groups, members = mesh.devices.shape
    mesh = jax.sharding.Mesh(
        mesh.devices.reshape(groups, members // 2, 2), ("group", "chip", "core")
    )
    in_specs = (
        P(("group", "chip", "core"), None),
        P(("group", "chip", "core"), None),
        P(),
        P(("group", "chip", "core")),
        P(("group", "chip", "core")),
        P(("group", "chip", "core")),
        P(("group", "chip", "core")),
    )
    out_specs = (
        P(("group", "chip", "core")),
        P(("group", "chip", "core"), None),
        P(("group", "chip", "core"), None),
        P(),
    )
    return jax.shard_map(body, mesh=mesh, in_specs=in_specs, out_specs=out_specs, check_vma=False)
```
